32 devices in a mesh: gz: 4 (over z), xy: 8 (over y, x, core).
Axes of the slice: x: 2, y: 2, z: 4, core: 2. Of those that a mesh axis runs over, the one named last changes fastest.
Arguments:
- tile_image: bfloat16 [4, 8, 4, 4, 2, 128], P('gz', 'xy'), may hold values from -6 to 6
- tile_target: bfloat16 [4, 8, 4, 3, 4, 2, 128], P('gz', 'xy'), may hold values from 0 to 1
- owner_counts: int32 [4, 8], P('gz', 'xy'), may hold values from 0 to 4, as said below
- tile_list: int32 [4, 8, 4], P('gz', 'xy'), may hold values from -1 to 15, as said below
- w_in: bfloat16 [27, 32], replicated, may hold values from -1.25 to 1.25
- w_res: bfloat16 [27, 32, 32], replicated, may hold values from -0.21875 to 0.21875
- w_down: bfloat16 [8, 64, 32], replicated, may hold values from -0.375 to 0.375
- w_mid: bfloat16 [27, 64, 64], replicated, may hold values from -0.15625 to 0.15625
- w_up: bfloat16 [8, 32, 64], replicated, may hold values from -0.75 to 0.75
- head_weight: bfloat16 [3, 32], replicated, may hold values from -1 to 1
Outputs:
- err_tiles: bfloat16 [4, 8, 4, 3, 4, 2, 128], P('gz', 'xy')
- grad_in: float32 [27, 32], replicated
- grad_res: float32 [27, 32, 32], replicated
- grad_down: float32 [8, 64, 32], replicated
- grad_mid: float32 [27, 64, 64], replicated
- grad_up: float32 [8, 32, 64], replicated
- head_weight_gradient: float32 [3, 32], replicated
The draws below stay inside these ranges and needn't reach their ends.
Inputs may be any that keep to these rules, and one draw needn't show every extreme that they name: `owner_counts`: in each depth row the counts add up to 16, and some owner of every row holds exactly 4 tiles. `tile_list`: in each depth row the live slots (s < owner_counts) name every position 0 to 15 exactly once; the other slots hold -1.
All inputs are finite; a program needn't handle non-finite values.
Results may differ from the reference program's by a relative error of at most 0.0046.
Values may be sent and summed in bfloat16 or wider, within the bound.
No kernel may reach another device: no remote copies, remote signals or barrier semaphores. Data moves between devices by JAX's collectives and lax.ppermute only.
A program may use at most 64 MiB of HBM per device.

```python
import jax
import jax.numpy as jnp
from jax import lax

CH0 = 32
CH1 = 64
CZ = 4
CY = 2
TX = 128
TPD = 2
MAXT = 4
TOT = 16
NZ = 16
NX = 2048
SLAB_VOXELS = 65536
N_GZ = 4
N_XY = 8


def owner_plan(key):
    base = jax.random.fold_in(key, 101)
    row_keys = jax.random.split(base, N_GZ)

    def one_row(row_key):
        key_order, key_delta, key_place = jax.random.split(row_key, 3)
        order = jax.random.permutation(key_order, N_XY)
        delta = jax.random.randint(key_delta, (N_XY // 2,), -TPD, TPD + 1)
        delta = delta.at[0].set(MAXT - TPD)
        counts = jnp.zeros((N_XY,), jnp.int32)
        counts = counts.at[order[0::2]].set(TPD + delta).at[order[1::2]].set(TPD - delta)
        places = jax.random.permutation(key_place, N_XY * TPD).astype(jnp.int32)
        offsets = jnp.cumsum(counts) - counts
        slots = jnp.arange(MAXT, dtype=jnp.int32)
        index = jnp.clip(offsets[:, None] + slots[None, :], 0, N_XY * TPD - 1)
        listing = jnp.where(slots[None, :] < counts[:, None], places[index], -1)
        return (counts.astype(jnp.int32), listing.astype(jnp.int32))
    return jax.vmap(one_row)(row_keys)


def draw_owner_counts(key, part):
    return owner_plan(key)[0]


def draw_tile_list(key, part):
    return owner_plan(key)[1]


def draw_tile_target(key, part):
    key_kind, key_rough = jax.random.split(jax.random.fold_in(key, 202))
    kind = jax.random.randint(key_kind, (N_GZ, N_XY, MAXT, 3, 1, 1, 1), 0, 2).astype(jnp.float32)
    rough = jax.random.uniform(key_rough, (N_GZ, N_XY, MAXT, 3, CZ, CY, TX), jnp.float32)
    width_part = 0.1
    high = 1.0 - width_part * rough
    low = width_part * rough
    return (kind * high + (1.0 - kind) * low).astype(jnp.bfloat16)


def steps_of(rng, dims, shards, least, top_value):
    factor_of = 1.0
    for axis_at, shards_of in shards:
        steps = jax.random.uniform(jax.random.fold_in(jax.random.fold_in(rng, 6), axis_at), (shards_of,), jnp.float32, least / len(shards), top_value / len(shards))
        factor_of = factor_of * jnp.repeat(jnp.exp(steps), dims[axis_at] // shards_of).reshape((-1,) + (1,) * (len(dims) - 1 - axis_at))
    return factor_of


def bell_draw(rng, extent, scale, limit, pieces=(), held_as=jnp.bfloat16):
    factor_of = steps_of(rng, extent, pieces, -0.22, 0.18) if pieces else 1.0
    values = jax.random.normal(rng, extent, jnp.float32) * scale * factor_of
    return jnp.minimum(jnp.maximum(values, -limit), limit).astype(held_as)


def setup_inputs(seed: int = 0) -> dict:
    splits = jax.random.split(jax.random.key(seed), 11)
    return {
        "tile_image": bell_draw(splits[0], (N_GZ, N_XY, MAXT, CZ, CY, TX), 1.0, 6.0, ((0, 4), (1, 8))),
        "tile_target": draw_tile_target(jax.random.fold_in(splits[10], 71), 0),
        "owner_counts": draw_owner_counts(jax.random.fold_in(splits[10], 71), 0),
        "tile_list": draw_tile_list(jax.random.fold_in(splits[10], 71), 0),
        "w_in": bell_draw(splits[4], (27, CH0), 27 ** -0.5, 1.25),
        "w_res": bell_draw(splits[5], (27, CH0, CH0), (27 * CH0) ** -0.5, 0.21875),
        "w_down": bell_draw(splits[6], (8, CH1, CH0), (8 * CH0) ** -0.5, 0.375),
        "w_mid": bell_draw(splits[7], (27, CH1, CH1), (27 * CH1) ** -0.5, 0.15625),
        "w_up": bell_draw(splits[8], (8, CH0, CH1), CH1 ** -0.5, 0.75),
        "head_weight": bell_draw(splits[9], (3, CH0), CH0 ** -0.5, 1.0),
    }


def convolve(field, weights):
    kernel = weights.reshape(3, 3, 3, weights.shape[1], weights.shape[2]).transpose(3, 4, 0, 1, 2)
    result = lax.conv_general_dilated(field[None], kernel, (1, 1, 1), ((1, 1), (1, 1), (1, 1)),
                                      dimension_numbers=("NCDHW", "OIDHW", "NCDHW"),
                                      preferred_element_type=jnp.float32)
    return result[0]


def flipped(weights):
    return jnp.transpose(weights[::-1], (0, 2, 1))


def tap_grads(grad, field):
    padded = jnp.pad(field, ((0, 0), (1, 1), (1, 1), (1, 1)))
    depth, height, width = grad.shape[1:]
    grad_f = grad.astype(jnp.float32)
    terms = []
    for tap in range(27):
        off_z, off_y, off_x = tap // 9, (tap // 3) % 3, tap % 3
        window = padded[:, off_z:off_z + depth, off_y:off_y + height, off_x:off_x + width].astype(jnp.float32)
        terms.append(jnp.einsum("ozyx,czyx->oc", grad_f, window))
    return jnp.stack(terms)


def strided(field, tap):
    return field[:, tap // 4::2, (tap // 2) % 2::2, tap % 2::2]


def alternate(parts):
    chans, depth, height, width = parts.shape[1:]
    return parts.reshape(2, 2, 2, chans, depth, height, width).transpose(3, 4, 0, 5, 1, 6, 2).reshape(
        chans, 2 * depth, 2 * height, 2 * width)


def selector(counts_row, list_row):
    live = jnp.arange(MAXT)[None, :] < counts_row[:, None]
    match = (list_row.reshape(-1)[None, :] == jnp.arange(TOT)[:, None]) & live.reshape(-1)[None, :]
    return match.astype(jnp.float32)


def reference(tile_image, tile_target, owner_counts, tile_list, w_in, w_res, w_down, w_mid, w_up, head_weight):
    single_float = jnp.float32
    brain_float_half = jnp.bfloat16
    hi = lax.Precision.HIGHEST
    image_rows = []
    target_rows = []
    selects = []
    for row in range(N_GZ):
        select = selector(owner_counts[row], tile_list[row])
        selects.append(select)
        flat_img = tile_image[row].reshape((N_XY * MAXT, CZ, CY, TX)).astype(single_float)
        flat_tgt = tile_target[row].reshape((N_XY * MAXT, 3, CZ, CY, TX)).astype(single_float)
        image_rows.append(jnp.tensordot(select, flat_img, axes=1, precision=hi))
        target_rows.append(jnp.tensordot(select, flat_tgt, axes=1, precision=hi))
    image = jnp.stack(image_rows).transpose(0, 2, 3, 1, 4).reshape(1, NZ, CY, NX).astype(brain_float_half)
    target = jnp.stack(target_rows).transpose(2, 0, 3, 4, 1, 5).reshape(3, NZ, CY, NX).astype(brain_float_half)

    h0 = jax.nn.relu(convolve(image, w_in[:, :, None])).astype(brain_float_half)
    h1 = jax.nn.relu(h0.astype(single_float) + convolve(h0, w_res)).astype(brain_float_half)
    down_sum = sum(jnp.einsum("oc,czyx->ozyx", w_down[tap].astype(single_float), strided(h1, tap).astype(single_float)) for tap in range(8))
    dfield = jax.nn.relu(down_sum).astype(brain_float_half)
    cfield = jax.nn.relu(dfield.astype(single_float) + convolve(dfield, w_mid)).astype(brain_float_half)
    upward = alternate(jnp.stack([jnp.einsum("oc,czyx->ozyx", w_up[tap].astype(single_float), cfield.astype(single_float)) for tap in range(8)]))
    signal_field = jax.nn.relu(h1.astype(single_float) + upward).astype(brain_float_half)
    logits = jnp.einsum("ac,czyx->azyx", head_weight.astype(single_float), signal_field.astype(single_float))
    affinity_map = jax.nn.sigmoid(logits)
    error_field = affinity_map - target.astype(single_float)
    err_out = error_field.astype(brain_float_half)

    tiles = err_out.reshape(3, N_GZ, CZ, CY, TOT, TX).transpose(1, 4, 0, 2, 3, 5).astype(single_float)
    slot_rows = []
    for row in range(N_GZ):
        placed = jnp.tensordot(selects[row].T, tiles[row], axes=1, precision=hi)
        slot_rows.append(placed.reshape(N_XY, MAXT, 3, CZ, CY, TX))
    err_tiles = jnp.stack(slot_rows).astype(brain_float_half)

    logit_gradient = (error_field * affinity_map * (1.0 - affinity_map) / SLAB_VOXELS).astype(brain_float_half)
    head_weight_gradient = jnp.einsum("mtnq,btnq->mb", logit_gradient.astype(single_float), signal_field.astype(single_float))
    gradient_total = jnp.einsum("jn,jbrq->nbrq", head_weight.astype(single_float), logit_gradient.astype(single_float))
    gsf = jnp.where(signal_field > 0, gradient_total, 0.0).astype(brain_float_half)
    grad_up = jnp.stack([jnp.einsum("ozyx,czyx->oc", strided(gsf, tap).astype(single_float), cfield.astype(single_float)) for tap in range(8)])
    gcoarse = sum(jnp.einsum("oc,ozyx->czyx", w_up[tap].astype(single_float), strided(gsf, tap).astype(single_float)) for tap in range(8))
    gquad = jnp.where(cfield > 0, gcoarse, 0.0).astype(brain_float_half)
    grad_mid = tap_grads(gquad, dfield)
    gdown = gquad.astype(single_float) + convolve(gquad, flipped(w_mid))
    gdd = jnp.where(dfield > 0, gdown, 0.0).astype(brain_float_half)
    grad_down = jnp.stack([jnp.einsum("ozyx,czyx->oc", gdd.astype(single_float), strided(h1, tap).astype(single_float)) for tap in range(8)])
    spread = alternate(jnp.stack([jnp.einsum("oc,ozyx->czyx", w_down[tap].astype(single_float), gdd.astype(single_float)) for tap in range(8)]))
    gres = jnp.where(h1 > 0, gsf.astype(single_float) + spread, 0.0).astype(brain_float_half)
    grad_res = tap_grads(gres, h0)
    gfirst = gres.astype(single_float) + convolve(gres, flipped(w_res))
    gact = jnp.where(h0 > 0, gfirst, 0.0).astype(brain_float_half)
    grad_in = tap_grads(gact, image)[:, :, 0]
    return (err_tiles, grad_in, grad_res, grad_down, grad_mid, grad_up, head_weight_gradient)
```

```python
import jax
import jax.numpy as jnp
from jax import lax
from jax.sharding import PartitionSpec as P

TPD = 2


def tree_sum(grads, axes):
    count = 1
    for axis in axes:
        count *= lax.axis_size(axis)
    if count & (count - 1):
        return lax.psum(grads, axes)
    flat = jnp.concatenate([g.reshape(-1) for g in grads])
    size = flat.shape[0]
    padded = -(-size // count) * count
    flat = jnp.pad(flat, (0, padded - size))
    index = lax.axis_index(axes[0])
    for axis in axes[1:]:
        index = index * lax.axis_size(axis) + lax.axis_index(axis)
    cur = flat
    step = 1
    while step < count:
        half = cur.shape[0] // 2
        upper = (index // step) % 2 == 1
        low, high = cur[:half], cur[half:]
        keep = jnp.where(upper, high, low)
        send = jnp.where(upper, low, high)
        pairs = [(i, i ^ step) for i in range(count)]
        cur = keep + lax.ppermute(send, axes, pairs)
        step *= 2
    step = count // 2
    while step >= 1:
        pairs = [(i, i ^ step) for i in range(count)]
        other = lax.ppermute(cur, axes, pairs)
        upper = (index // step) % 2 == 1
        cur = jnp.where(upper, jnp.concatenate([other, cur]), jnp.concatenate([cur, other]))
        step //= 2
    out = []
    offset = 0
    for g in grads:
        out.append(cur[offset : offset + g.size].reshape(g.shape))
        offset += g.size
    return tuple(out)


def with_halo(cells, sides, width):
    for axis, dim in sides:
        count = lax.axis_size(axis)
        ends = count - 1
        head = lax.slice_in_dim(cells, 0, width, axis=dim)
        tail = lax.slice_in_dim(cells, cells.shape[dim] - width, cells.shape[dim], axis=dim)
        cells = jnp.concatenate(
            [
                lax.ppermute(tail, axis, [(i, (i + 1) % count) for i in range(ends)]),
                cells,
                lax.ppermute(head, axis, [((i + 1) % count, i) for i in range(ends)]),
            ],
            axis=dim,
        )
    return cells


def framed(field):
    padded = with_halo(field, (("gz", 1), ("xy", 3)), 1)
    return jnp.pad(padded, ((0, 0), (0, 0), (1, 1), (0, 0)))


def convolve(padded, weights):
    depth = padded.shape[1] - 2
    height = padded.shape[2] - 2
    width = padded.shape[3] - 2
    total = None
    for tap in range(27):
        off_z, off_y, off_x = (tap // 9, tap // 3 % 3, tap % 3)
        window = padded[:, off_z : off_z + depth, off_y : off_y + height, off_x : off_x + width]
        term = jnp.einsum("oc,czyx->ozyx", weights[tap], window, preferred_element_type=jnp.float32)
        total = term if total is None else total + term
    return total


def tap_grads(grad, padded):
    depth, height, width = grad.shape[1:]
    terms = []
    for tap in range(27):
        off_z, off_y, off_x = (tap // 9, tap // 3 % 3, tap % 3)
        window = padded[:, off_z : off_z + depth, off_y : off_y + height, off_x : off_x + width]
        terms.append(jnp.einsum("ozyx,czyx->oc", grad, window, preferred_element_type=jnp.float32))
    return jnp.stack(terms)


def flipped(weights):
    return jnp.transpose(weights[::-1], (0, 2, 1))


def strided(field, tap):
    return field[:, tap // 4 :: 2, tap // 2 % 2 :: 2, tap % 2 :: 2]


def alternate(parts):
    chans, depth, height, width = parts.shape[1:]
    return (
        parts.reshape(2, 2, 2, chans, depth, height, width)
        .transpose(3, 4, 0, 5, 1, 6, 2)
        .reshape(chans, 2 * depth, 2 * height, 2 * width)
    )


def local(
    tile_image, tile_target, owner_counts, tile_list, w_in, w_res, w_down, w_mid, w_up, head_weight
):
    single_float = jnp.float32
    brain_float_half = jnp.bfloat16
    ranks = lax.axis_size("xy")
    layers = lax.axis_size("gz")
    column = lax.axis_index("xy")
    slots = tile_list.shape[2]
    depth, height, width = (tile_image.shape[3], tile_image.shape[4], tile_image.shape[5])
    per_dev = TPD
    total_tiles = ranks * per_dev
    slot_list = tile_list[0, 0]
    live = jnp.arange(slots) < owner_counts[0, 0]
    select = ((slot_list[None, :] == jnp.arange(total_tiles)[:, None]) & live[None, :]).astype(
        brain_float_half
    )
    payload = jnp.concatenate([tile_image[0, 0][:, None], tile_target[0, 0]], axis=1)
    outgoing = jnp.einsum("ps,sazyx->pazyx", select, payload, preferred_element_type=single_float)
    outgoing = outgoing.astype(brain_float_half).reshape((ranks, per_dev) + payload.shape[1:])
    incoming = lax.all_to_all(outgoing, "xy", 0, 0, tiled=True)
    mine = jnp.sum(incoming.astype(single_float), axis=0).astype(brain_float_half)
    mine_img = mine[:, 0]
    mine_tgt = mine[:, 1:]
    image = mine_img.transpose(1, 2, 0, 3).reshape(1, depth, height, per_dev * width)
    target = mine_tgt.transpose(1, 2, 3, 0, 4).reshape(3, depth, height, per_dev * width)
    voxel_cells = depth * height * per_dev * width * ranks * layers
    image_pad = framed(image)
    h0 = jax.nn.relu(convolve(image_pad, w_in[:, :, None])).astype(brain_float_half)
    h0_pad = framed(h0)
    h1 = jax.nn.relu(h0.astype(single_float) + convolve(h0_pad, w_res)).astype(brain_float_half)
    down_sum = None
    for tap in range(8):
        term = jnp.einsum(
            "oc,czyx->ozyx", w_down[tap], strided(h1, tap), preferred_element_type=single_float
        )
        down_sum = term if down_sum is None else down_sum + term
    dfield = jax.nn.relu(down_sum).astype(brain_float_half)
    dfield_pad = framed(dfield)
    cfield = jax.nn.relu(dfield.astype(single_float) + convolve(dfield_pad, w_mid)).astype(
        brain_float_half
    )
    upward = alternate(
        jnp.stack(
            [
                jnp.einsum("oc,czyx->ozyx", w_up[tap], cfield, preferred_element_type=single_float)
                for tap in range(8)
            ]
        )
    )
    signal_field = jax.nn.relu(h1.astype(single_float) + upward).astype(brain_float_half)
    logits = jnp.einsum(
        "ac,czyx->azyx", head_weight, signal_field, preferred_element_type=single_float
    )
    affinity_map = jax.nn.sigmoid(logits)
    error_field = affinity_map - target.astype(single_float)
    err_out = error_field.astype(brain_float_half)
    err_local = err_out.reshape(3, depth, height, per_dev, width).transpose(3, 0, 1, 2, 4)
    sending = jnp.broadcast_to(err_local[None], (ranks,) + err_local.shape)
    returned = lax.all_to_all(sending, "xy", split_axis=0, concat_axis=0, tiled=True)
    returned = returned.reshape((total_tiles, 3, depth, height, width))
    err_tiles = jnp.einsum(
        "ps,pazyx->sazyx", select, returned, preferred_element_type=single_float
    ).astype(brain_float_half)[None, None]
    logit_gradient = (error_field * affinity_map * (1.0 - affinity_map) / voxel_cells).astype(
        brain_float_half
    )
    head_weight_gradient = jnp.einsum(
        "mtnq,btnq->mb", logit_gradient, signal_field, preferred_element_type=single_float
    )
    gradient_total = jnp.einsum(
        "jn,jbrq->nbrq", head_weight, logit_gradient, preferred_element_type=single_float
    )
    gsf = jnp.where(signal_field > 0, gradient_total, 0.0).astype(brain_float_half)
    grad_up = jnp.stack(
        [
            jnp.einsum(
                "ozyx,czyx->oc", strided(gsf, tap), cfield, preferred_element_type=single_float
            )
            for tap in range(8)
        ]
    )
    gcoarse = None
    for tap in range(8):
        term = jnp.einsum(
            "oc,ozyx->czyx", w_up[tap], strided(gsf, tap), preferred_element_type=single_float
        )
        gcoarse = term if gcoarse is None else gcoarse + term
    gquad = jnp.where(cfield > 0, gcoarse, 0.0).astype(brain_float_half)
    grad_mid = tap_grads(gquad, dfield_pad)
    gdown = gquad.astype(single_float) + convolve(framed(gquad), flipped(w_mid))
    gdd = jnp.where(dfield > 0, gdown, 0.0).astype(brain_float_half)
    grad_down = jnp.stack(
        [
            jnp.einsum("ozyx,czyx->oc", gdd, strided(h1, tap), preferred_element_type=single_float)
            for tap in range(8)
        ]
    )
    spread = alternate(
        jnp.stack(
            [
                jnp.einsum("oc,ozyx->czyx", w_down[tap], gdd, preferred_element_type=single_float)
                for tap in range(8)
            ]
        )
    )
    gres = jnp.where(h1 > 0, gsf.astype(single_float) + spread, 0.0).astype(brain_float_half)
    grad_res = tap_grads(gres, h0_pad)
    gfirst = gres.astype(single_float) + convolve(framed(gres), flipped(w_res))
    gact = jnp.where(h0 > 0, gfirst, 0.0).astype(brain_float_half)
    grad_in = tap_grads(gact, image_pad)[:, :, 0]
    summed = tree_sum(
        (grad_in, grad_res, grad_down, grad_mid, grad_up, head_weight_gradient), ("gz", "xy")
    )
    return (err_tiles, summed[0], summed[1], summed[2], summed[3], summed[4], summed[5])


def solution(mesh):
    return jax.shard_map(
        local,
        mesh=mesh,
        in_specs=(
            P("gz", "xy", None, None, None, None),
            P("gz", "xy", None, None, None, None, None),
            P("gz", "xy"),
            P("gz", "xy", None),
            P(),
            P(),
            P(),
            P(),
            P(),
            P(),
        ),
        out_specs=(P("gz", "xy", None, None, None, None, None), P(), P(), P(), P(), P(), P()),
        check_vma=False,
    )
```

```python
import jax
import jax.numpy as jnp
from jax import lax
from jax.sharding import PartitionSpec as P

TPD = 2


def tree_sum(grads, axes):
    count = 1
    for axis in axes:
        count *= lax.axis_size(axis)
    if count & (count - 1):
        return lax.psum(grads, axes)
    flat = jnp.concatenate([g.reshape(-1) for g in grads])
    size = flat.shape[0]
    padded = -(-size // count) * count
    flat = jnp.pad(flat, (0, padded - size))
    index = lax.axis_index(axes[0])
    for axis in axes[1:]:
        index = index * lax.axis_size(axis) + lax.axis_index(axis)
    cur = flat
    step = 1
    while step < count:
        half = cur.shape[0] // 2
        upper = (index // step) % 2 == 1
        low, high = cur[:half], cur[half:]
        keep = jnp.where(upper, high, low)
        send = jnp.where(upper, low, high)
        pairs = [(i, i ^ step) for i in range(count)]
        cur = keep + lax.ppermute(send, axes, pairs)
        step *= 2
    step = count // 2
    while step >= 1:
        pairs = [(i, i ^ step) for i in range(count)]
        other = lax.ppermute(cur, axes, pairs)
        upper = (index // step) % 2 == 1
        cur = jnp.where(upper, jnp.concatenate([other, cur]), jnp.concatenate([cur, other]))
        step //= 2
    out = []
    offset = 0
    for g in grads:
        out.append(cur[offset : offset + g.size].reshape(g.shape))
        offset += g.size
    return tuple(out)


def inside(shape, first_z, first_x, total_z, total_x):
    zs = first_z + jnp.arange(shape[1])
    xs = first_x + jnp.arange(shape[3])
    keep_z = (zs >= 0) & (zs < total_z)
    keep_x = (xs >= 0) & (xs < total_x)
    return (keep_z[:, None] & keep_x[None, :])[None, :, None, :]


def with_halo(cells, sides, width):
    for axis, dim in sides:
        count = lax.axis_size(axis)
        ends = count - 1
        head = lax.slice_in_dim(cells, 0, width, axis=dim)
        tail = lax.slice_in_dim(cells, cells.shape[dim] - width, cells.shape[dim], axis=dim)
        cells = jnp.concatenate(
            [
                lax.ppermute(tail, axis, [(i, (i + 1) % count) for i in range(ends)]),
                cells,
                lax.ppermute(head, axis, [((i + 1) % count, i) for i in range(ends)]),
            ],
            axis=dim,
        )
    return cells


def framed(field):
    padded = with_halo(field, (("gz", 1), ("xy", 3)), 1)
    return jnp.pad(padded, ((0, 0), (0, 0), (1, 1), (0, 0)))


def convolve(padded, weights):
    depth = padded.shape[1] - 2
    height = padded.shape[2] - 2
    width = padded.shape[3] - 2
    total = None
    for tap in range(27):
        off_z, off_y, off_x = (tap // 9, tap // 3 % 3, tap % 3)
        window = padded[:, off_z : off_z + depth, off_y : off_y + height, off_x : off_x + width]
        term = jnp.einsum("oc,czyx->ozyx", weights[tap], window, preferred_element_type=jnp.float32)
        total = term if total is None else total + term
    return total


def tap_grads(grad, padded):
    depth, height, width = grad.shape[1:]
    terms = []
    for tap in range(27):
        off_z, off_y, off_x = (tap // 9, tap // 3 % 3, tap % 3)
        window = padded[:, off_z : off_z + depth, off_y : off_y + height, off_x : off_x + width]
        terms.append(jnp.einsum("ozyx,czyx->oc", grad, window, preferred_element_type=jnp.float32))
    return jnp.stack(terms)


def flipped(weights):
    return jnp.transpose(weights[::-1], (0, 2, 1))


def strided(field, tap):
    return field[:, tap // 4 :: 2, tap // 2 % 2 :: 2, tap % 2 :: 2]


def alternate(parts):
    chans, depth, height, width = parts.shape[1:]
    return (
        parts.reshape(2, 2, 2, chans, depth, height, width)
        .transpose(3, 4, 0, 5, 1, 6, 2)
        .reshape(chans, 2 * depth, 2 * height, 2 * width)
    )


def local(
    tile_image, tile_target, owner_counts, tile_list, w_in, w_res, w_down, w_mid, w_up, head_weight
):
    single_float = jnp.float32
    brain_float_half = jnp.bfloat16
    ranks = lax.axis_size("xy")
    layers = lax.axis_size("gz")
    column = lax.axis_index("xy")
    slots = tile_list.shape[2]
    depth, height, width = (tile_image.shape[3], tile_image.shape[4], tile_image.shape[5])
    per_dev = TPD
    total_tiles = ranks * per_dev
    slot_list = tile_list[0, 0]
    live = jnp.arange(slots) < owner_counts[0, 0]
    select = ((slot_list[None, :] == jnp.arange(total_tiles)[:, None]) & live[None, :]).astype(
        brain_float_half
    )
    payload = jnp.concatenate([tile_image[0, 0][:, None], tile_target[0, 0]], axis=1)
    outgoing = jnp.einsum("ps,sazyx->pazyx", select, payload, preferred_element_type=single_float)
    outgoing = outgoing.astype(brain_float_half).reshape((ranks, per_dev) + payload.shape[1:])
    incoming = lax.all_to_all(outgoing, "xy", 0, 0, tiled=True)
    mine = jnp.sum(incoming.astype(single_float), axis=0).astype(brain_float_half)
    mine_img = mine[:, 0]
    mine_tgt = mine[:, 1:]
    image = mine_img.transpose(1, 2, 0, 3).reshape(1, depth, height, per_dev * width)
    target = mine_tgt.transpose(1, 2, 3, 0, 4).reshape(3, depth, height, per_dev * width)
    voxel_cells = depth * height * per_dev * width * ranks * layers
    block_z = lax.axis_index("gz") * depth
    block_x = column * per_dev * width
    image_wide = with_halo(image, (("gz", 1), ("xy", 3)), 4)
    image_wide = jnp.pad(image_wide, ((0, 0), (0, 0), (1, 1), (0, 0)))
    image_pad = image_wide[:, 3:-3, :, 3:-3]
    h0_wide = jax.nn.relu(convolve(image_wide, w_in[:, :, None]))
    h0_wide = jnp.where(
        inside(h0_wide.shape, block_z - 3, block_x - 3, depth * layers, per_dev * width * ranks),
        h0_wide,
        0.0,
    ).astype(brain_float_half)
    h0_wide = jnp.pad(h0_wide, ((0, 0), (0, 0), (1, 1), (0, 0)))
    h0 = h0_wide[:, 3:-3, 1:-1, 3:-3]
    h0_pad = h0_wide[:, 2:-2, :, 2:-2]
    h1_wide = jax.nn.relu(
        h0_wide[:, 1:-1, 1:-1, 1:-1].astype(single_float) + convolve(h0_wide, w_res)
    ).astype(brain_float_half)
    h1 = h1_wide[:, 2:-2, :, 2:-2]
    down_sum = None
    for tap in range(8):
        term = jnp.einsum(
            "oc,czyx->ozyx", w_down[tap], strided(h1_wide, tap), preferred_element_type=single_float
        )
        down_sum = term if down_sum is None else down_sum + term
    d_wide = jnp.where(
        inside(
            down_sum.shape,
            block_z // 2 - 1,
            block_x // 2 - 1,
            depth * layers // 2,
            per_dev * width * ranks // 2,
        ),
        jax.nn.relu(down_sum),
        0.0,
    ).astype(brain_float_half)
    dfield = d_wide[:, 1:-1, :, 1:-1]
    dfield_pad = jnp.pad(d_wide, ((0, 0), (0, 0), (1, 1), (0, 0)))
    cfield = jax.nn.relu(dfield.astype(single_float) + convolve(dfield_pad, w_mid)).astype(
        brain_float_half
    )
    upward = alternate(
        jnp.stack(
            [
                jnp.einsum("oc,czyx->ozyx", w_up[tap], cfield, preferred_element_type=single_float)
                for tap in range(8)
            ]
        )
    )
    signal_field = jax.nn.relu(h1.astype(single_float) + upward).astype(brain_float_half)
    logits = jnp.einsum(
        "ac,czyx->azyx", head_weight, signal_field, preferred_element_type=single_float
    )
    affinity_map = jax.nn.sigmoid(logits)
    error_field = affinity_map - target.astype(single_float)
    err_out = error_field.astype(brain_float_half)
    err_local = err_out.reshape(3, depth, height, per_dev, width).transpose(3, 0, 1, 2, 4)
    sending = jnp.broadcast_to(err_local[None], (ranks,) + err_local.shape)
    returned = lax.all_to_all(sending, "xy", split_axis=0, concat_axis=0, tiled=True)
    returned = returned.reshape((total_tiles, 3, depth, height, width))
    err_tiles = jnp.einsum(
        "ps,pazyx->sazyx", select, returned, preferred_element_type=single_float
    ).astype(brain_float_half)[None, None]
    logit_gradient = (error_field * affinity_map * (1.0 - affinity_map) / voxel_cells).astype(
        brain_float_half
    )
    head_weight_gradient = jnp.einsum(
        "mtnq,btnq->mb", logit_gradient, signal_field, preferred_element_type=single_float
    )
    gradient_total = jnp.einsum(
        "jn,jbrq->nbrq", head_weight, logit_gradient, preferred_element_type=single_float
    )
    gsf = jnp.where(signal_field > 0, gradient_total, 0.0).astype(brain_float_half)
    grad_up = jnp.stack(
        [
            jnp.einsum(
                "ozyx,czyx->oc", strided(gsf, tap), cfield, preferred_element_type=single_float
            )
            for tap in range(8)
        ]
    )
    gcoarse = None
    for tap in range(8):
        term = jnp.einsum(
            "oc,ozyx->czyx", w_up[tap], strided(gsf, tap), preferred_element_type=single_float
        )
        gcoarse = term if gcoarse is None else gcoarse + term
    gquad = jnp.where(cfield > 0, gcoarse, 0.0).astype(brain_float_half)
    grad_mid = tap_grads(gquad, dfield_pad)
    gdown = gquad.astype(single_float) + convolve(framed(gquad), flipped(w_mid))
    gdd = jnp.where(dfield > 0, gdown, 0.0).astype(brain_float_half)
    grad_down = jnp.stack(
        [
            jnp.einsum("ozyx,czyx->oc", gdd, strided(h1, tap), preferred_element_type=single_float)
            for tap in range(8)
        ]
    )
    spread = alternate(
        jnp.stack(
            [
                jnp.einsum("oc,ozyx->czyx", w_down[tap], gdd, preferred_element_type=single_float)
                for tap in range(8)
            ]
        )
    )
    gres = jnp.where(h1 > 0, gsf.astype(single_float) + spread, 0.0).astype(brain_float_half)
    grad_res = tap_grads(gres, h0_pad)
    gfirst = gres.astype(single_float) + convolve(framed(gres), flipped(w_res))
    gact = jnp.where(h0 > 0, gfirst, 0.0).astype(brain_float_half)
    grad_in = tap_grads(gact, image_pad)[:, :, 0]
    summed = tree_sum(
        (grad_in, grad_res, grad_down, grad_mid, grad_up, head_weight_gradient), ("gz", "xy")
    )
    return (err_tiles, summed[0], summed[1], summed[2], summed[3], summed[4], summed[5])


def solution(mesh):
    return jax.shard_map(
        local,
        mesh=mesh,
        in_specs=(
            P("gz", "xy", None, None, None, None),
            P("gz", "xy", None, None, None, None, None),
            P("gz", "xy"),
            P("gz", "xy", None),
            P(),
            P(),
            P(),
            P(),
            P(),
            P(),
        ),
        out_specs=(P("gz", "xy", None, None, None, None, None), P(), P(), P(), P(), P(), P()),
        check_vma=False,
    )
```

```python
import jax
import jax.numpy as jnp
from jax import lax
from jax.sharding import PartitionSpec as P

TPD = 2


def tree_sum(grads, axes):
    count = 1
    for axis in axes:
        count *= lax.axis_size(axis)
    if count & (count - 1):
        return lax.psum(grads, axes)
    flat = jnp.concatenate([g.reshape(-1) for g in grads])
    size = flat.shape[0]
    padded = -(-size // count) * count
    flat = jnp.pad(flat, (0, padded - size))
    index = lax.axis_index(axes[0])
    for axis in axes[1:]:
        index = index * lax.axis_size(axis) + lax.axis_index(axis)
    cur = flat
    step = 1
    while step < count:
        half = cur.shape[0] // 2
        upper = (index // step) % 2 == 1
        low, high = cur[:half], cur[half:]
        keep = jnp.where(upper, high, low)
        send = jnp.where(upper, low, high)
        pairs = [(i, i ^ step) for i in range(count)]
        cur = keep + lax.ppermute(send, axes, pairs)
        step *= 2
    step = count // 2
    while step >= 1:
        pairs = [(i, i ^ step) for i in range(count)]
        other = lax.ppermute(cur, axes, pairs)
        upper = (index // step) % 2 == 1
        cur = jnp.where(upper, jnp.concatenate([other, cur]), jnp.concatenate([cur, other]))
        step //= 2
    out = []
    offset = 0
    for g in grads:
        out.append(cur[offset : offset + g.size].reshape(g.shape))
        offset += g.size
    return tuple(out)


def inside(shape, first_z, first_x, total_z, total_x):
    zs = first_z + jnp.arange(shape[1])
    xs = first_x + jnp.arange(shape[3])
    keep_z = (zs >= 0) & (zs < total_z)
    keep_x = (xs >= 0) & (xs < total_x)
    return (keep_z[:, None] & keep_x[None, :])[None, :, None, :]


def with_halo(cells, sides, width):
    for axis, dim in sides:
        count = lax.axis_size(axis)
        ends = count - 1
        head = lax.slice_in_dim(cells, 0, width, axis=dim)
        tail = lax.slice_in_dim(cells, cells.shape[dim] - width, cells.shape[dim], axis=dim)
        cells = jnp.concatenate(
            [
                lax.ppermute(tail, axis, [(i, (i + 1) % count) for i in range(ends)]),
                cells,
                lax.ppermute(head, axis, [((i + 1) % count, i) for i in range(ends)]),
            ],
            axis=dim,
        )
    return cells


def framed(field):
    padded = with_halo(field, (("gz", 1), ("xy", 3)), 1)
    return jnp.pad(padded, ((0, 0), (0, 0), (1, 1), (0, 0)))


def convolve(padded, weights):
    depth = padded.shape[1] - 2
    height = padded.shape[2] - 2
    width = padded.shape[3] - 2
    total = None
    for tap in range(27):
        off_z, off_y, off_x = (tap // 9, tap // 3 % 3, tap % 3)
        window = padded[:, off_z : off_z + depth, off_y : off_y + height, off_x : off_x + width]
        term = jnp.einsum("oc,czyx->ozyx", weights[tap], window, preferred_element_type=jnp.float32)
        total = term if total is None else total + term
    return total


def tap_grads(grad, padded):
    depth, height, width = grad.shape[1:]
    terms = []
    for tap in range(27):
        off_z, off_y, off_x = (tap // 9, tap // 3 % 3, tap % 3)
        window = padded[:, off_z : off_z + depth, off_y : off_y + height, off_x : off_x + width]
        terms.append(jnp.einsum("ozyx,czyx->oc", grad, window, preferred_element_type=jnp.float32))
    return jnp.stack(terms)


def flipped(weights):
    return jnp.transpose(weights[::-1], (0, 2, 1))


def strided(field, tap):
    return field[:, tap // 4 :: 2, tap // 2 % 2 :: 2, tap % 2 :: 2]


def parity(field):
    chans, depth, height, width = field.shape
    return field.reshape(chans, depth // 2, 2, height // 2, 2, width // 2, 2)


def unparity(cube):
    shape = cube.shape
    return cube.reshape(shape[0], shape[1] * 2, shape[3] * 2, shape[5] * 2)


def alternate(parts):
    chans, depth, height, width = parts.shape[1:]
    return (
        parts.reshape(2, 2, 2, chans, depth, height, width)
        .transpose(3, 4, 0, 5, 1, 6, 2)
        .reshape(chans, 2 * depth, 2 * height, 2 * width)
    )


def local(
    tile_image, tile_target, owner_counts, tile_list, w_in, w_res, w_down, w_mid, w_up, head_weight
):
    single_float = jnp.float32
    brain_float_half = jnp.bfloat16
    ranks = lax.axis_size("xy")
    layers = lax.axis_size("gz")
    column = lax.axis_index("xy")
    slots = tile_list.shape[2]
    depth, height, width = (tile_image.shape[3], tile_image.shape[4], tile_image.shape[5])
    per_dev = TPD
    total_tiles = ranks * per_dev
    slot_list = tile_list[0, 0]
    live = jnp.arange(slots) < owner_counts[0, 0]
    select = ((slot_list[None, :] == jnp.arange(total_tiles)[:, None]) & live[None, :]).astype(
        brain_float_half
    )
    payload = jnp.concatenate([tile_image[0, 0][:, None], tile_target[0, 0]], axis=1)
    outgoing = jnp.einsum("ps,sazyx->pazyx", select, payload, preferred_element_type=single_float)
    outgoing = outgoing.astype(brain_float_half).reshape((ranks, per_dev) + payload.shape[1:])
    incoming = lax.all_to_all(outgoing, "xy", 0, 0, tiled=True)
    mine = jnp.sum(incoming.astype(single_float), axis=0).astype(brain_float_half)
    mine_img = mine[:, 0]
    mine_tgt = mine[:, 1:]
    image = mine_img.transpose(1, 2, 0, 3).reshape(1, depth, height, per_dev * width)
    target = mine_tgt.transpose(1, 2, 3, 0, 4).reshape(3, depth, height, per_dev * width)
    voxel_cells = depth * height * per_dev * width * ranks * layers
    block_z = lax.axis_index("gz") * depth
    block_x = column * per_dev * width
    image_wide = with_halo(image, (("gz", 1), ("xy", 3)), 4)
    image_wide = jnp.pad(image_wide, ((0, 0), (0, 0), (1, 1), (0, 0)))
    image_pad = image_wide[:, 3:-3, :, 3:-3]
    h0_wide = jax.nn.relu(convolve(image_wide, w_in[:, :, None]))
    h0_wide = jnp.where(
        inside(h0_wide.shape, block_z - 3, block_x - 3, depth * layers, per_dev * width * ranks),
        h0_wide,
        0.0,
    ).astype(brain_float_half)
    h0_wide = jnp.pad(h0_wide, ((0, 0), (0, 0), (1, 1), (0, 0)))
    h0 = h0_wide[:, 3:-3, 1:-1, 3:-3]
    h0_pad = h0_wide[:, 2:-2, :, 2:-2]
    h1_wide = jax.nn.relu(
        h0_wide[:, 1:-1, 1:-1, 1:-1].astype(single_float) + convolve(h0_wide, w_res)
    ).astype(brain_float_half)
    h1 = h1_wide[:, 2:-2, :, 2:-2]
    down_cube = w_down.reshape((2, 2, 2) + w_down.shape[1:])
    up_cube = w_up.reshape((2, 2, 2) + w_up.shape[1:])
    down_sum = jnp.einsum(
        "abeoc,czaybxe->ozyx", down_cube, parity(h1_wide), preferred_element_type=single_float
    )
    d_wide = jnp.where(
        inside(
            down_sum.shape,
            block_z // 2 - 1,
            block_x // 2 - 1,
            depth * layers // 2,
            per_dev * width * ranks // 2,
        ),
        jax.nn.relu(down_sum),
        0.0,
    ).astype(brain_float_half)
    dfield = d_wide[:, 1:-1, :, 1:-1]
    dfield_pad = jnp.pad(d_wide, ((0, 0), (0, 0), (1, 1), (0, 0)))
    cfield = jax.nn.relu(dfield.astype(single_float) + convolve(dfield_pad, w_mid)).astype(
        brain_float_half
    )
    upward = unparity(
        jnp.einsum("abeoc,czyx->ozaybxe", up_cube, cfield, preferred_element_type=single_float)
    )
    signal_field = jax.nn.relu(h1.astype(single_float) + upward).astype(brain_float_half)
    logits = jnp.einsum(
        "ac,czyx->azyx", head_weight, signal_field, preferred_element_type=single_float
    )
    affinity_map = jax.nn.sigmoid(logits)
    error_field = affinity_map - target.astype(single_float)
    err_out = error_field.astype(brain_float_half)
    err_local = err_out.reshape(3, depth, height, per_dev, width).transpose(3, 0, 1, 2, 4)
    sending = jnp.broadcast_to(err_local[None], (ranks,) + err_local.shape)
    returned = lax.all_to_all(sending, "xy", split_axis=0, concat_axis=0, tiled=True)
    returned = returned.reshape((total_tiles, 3, depth, height, width))
    err_tiles = jnp.einsum(
        "ps,pazyx->sazyx", select, returned, preferred_element_type=single_float
    ).astype(brain_float_half)[None, None]
    logit_gradient = (error_field * affinity_map * (1.0 - affinity_map) / voxel_cells).astype(
        brain_float_half
    )
    head_weight_gradient = jnp.einsum(
        "mtnq,btnq->mb", logit_gradient, signal_field, preferred_element_type=single_float
    )
    gradient_total = jnp.einsum(
        "jn,jbrq->nbrq", head_weight, logit_gradient, preferred_element_type=single_float
    )
    gsf = jnp.where(signal_field > 0, gradient_total, 0.0).astype(brain_float_half)
    gs_cube = parity(gsf)
    grad_up = jnp.einsum(
        "ozaybxe,czyx->abeoc", gs_cube, cfield, preferred_element_type=single_float
    ).reshape(w_up.shape)
    gcoarse = jnp.einsum("abeoc,ozaybxe->czyx", up_cube, gs_cube, preferred_element_type=single_float)
    gquad = jnp.where(cfield > 0, gcoarse, 0.0).astype(brain_float_half)
    grad_mid = tap_grads(gquad, dfield_pad)
    gdown = gquad.astype(single_float) + convolve(framed(gquad), flipped(w_mid))
    gdd = jnp.where(dfield > 0, gdown, 0.0).astype(brain_float_half)
    grad_down = jnp.einsum(
        "ozyx,czaybxe->abeoc", gdd, parity(h1), preferred_element_type=single_float
    ).reshape(w_down.shape)
    spread = unparity(
        jnp.einsum("abeoc,ozyx->czaybxe", down_cube, gdd, preferred_element_type=single_float)
    )
    gres = jnp.where(h1 > 0, gsf.astype(single_float) + spread, 0.0).astype(brain_float_half)
    grad_res = tap_grads(gres, h0_pad)
    gfirst = gres.astype(single_float) + convolve(framed(gres), flipped(w_res))
    gact = jnp.where(h0 > 0, gfirst, 0.0).astype(brain_float_half)
    grad_in = tap_grads(gact, image_pad)[:, :, 0]
    summed = tree_sum(
        (grad_in, grad_res, grad_down, grad_mid, grad_up, head_weight_gradient), ("gz", "xy")
    )
    return (err_tiles, summed[0], summed[1], summed[2], summed[3], summed[4], summed[5])


def solution(mesh):
    return jax.shard_map(
        local,
        mesh=mesh,
        in_specs=(
            P("gz", "xy", None, None, None, None),
            P("gz", "xy", None, None, None, None, None),
            P("gz", "xy"),
            P("gz", "xy", None),
            P(),
            P(),
            P(),
            P(),
            P(),
            P(),
        ),
        out_specs=(P("gz", "xy", None, None, None, None, None), P(), P(), P(), P(), P(), P()),
        check_vma=False,
    )
```

```python
import jax
import jax.numpy as jnp
from jax import lax
from jax.sharding import PartitionSpec as P

TPD = 2


def tree_sum(grads, axes):
    count = 1
    for axis in axes:
        count *= lax.axis_size(axis)
    if count & (count - 1):
        return lax.psum(grads, axes)
    flat = jnp.concatenate([g.reshape(-1) for g in grads])
    size = flat.shape[0]
    padded = -(-size // count) * count
    flat = jnp.pad(flat, (0, padded - size))
    index = lax.axis_index(axes[0])
    for axis in axes[1:]:
        index = index * lax.axis_size(axis) + lax.axis_index(axis)
    cur = flat
    step = 1
    while step < count:
        half = cur.shape[0] // 2
        upper = (index // step) % 2 == 1
        low, high = cur[:half], cur[half:]
        keep = jnp.where(upper, high, low)
        send = jnp.where(upper, low, high)
        pairs = [(i, i ^ step) for i in range(count)]
        cur = keep + lax.ppermute(send, axes, pairs)
        step *= 2
    step = count // 2
    while step >= 1:
        pairs = [(i, i ^ step) for i in range(count)]
        other = lax.ppermute(cur, axes, pairs)
        upper = (index // step) % 2 == 1
        cur = jnp.where(upper, jnp.concatenate([other, cur]), jnp.concatenate([cur, other]))
        step //= 2
    out = []
    offset = 0
    for g in grads:
        out.append(cur[offset : offset + g.size].reshape(g.shape))
        offset += g.size
    return tuple(out)


def inside(shape, first_z, first_x, total_z, total_x):
    zs = first_z + jnp.arange(shape[1])
    xs = first_x + jnp.arange(shape[3])
    keep_z = (zs >= 0) & (zs < total_z)
    keep_x = (xs >= 0) & (xs < total_x)
    return (keep_z[:, None] & keep_x[None, :])[None, :, None, :]


def with_halo(cells, sides, width):
    for axis, dim in sides:
        count = lax.axis_size(axis)
        ends = count - 1
        head = lax.slice_in_dim(cells, 0, width, axis=dim)
        tail = lax.slice_in_dim(cells, cells.shape[dim] - width, cells.shape[dim], axis=dim)
        cells = jnp.concatenate(
            [
                lax.ppermute(tail, axis, [(i, (i + 1) % count) for i in range(ends)]),
                cells,
                lax.ppermute(head, axis, [((i + 1) % count, i) for i in range(ends)]),
            ],
            axis=dim,
        )
    return cells


def framed(field):
    padded = with_halo(field, (("gz", 1), ("xy", 3)), 1)
    return jnp.pad(padded, ((0, 0), (0, 0), (1, 1), (0, 0)))


def windows(padded):
    depth = padded.shape[1] - 2
    height = padded.shape[2] - 2
    width = padded.shape[3] - 2
    cols = []
    for tap in range(27):
        off_z, off_y, off_x = (tap // 9, tap // 3 % 3, tap % 3)
        cols.append(
            padded[:, off_z : off_z + depth, off_y : off_y + height, off_x : off_x + width]
        )
    return jnp.stack(cols)


def convolve(padded, weights):
    return jnp.einsum(
        "toc,tczyx->ozyx", weights, windows(padded), preferred_element_type=jnp.float32
    )


def tap_grads(grad, padded):
    return jnp.einsum(
        "ozyx,tczyx->toc", grad, windows(padded), preferred_element_type=jnp.float32
    )


def flipped(weights):
    return jnp.transpose(weights[::-1], (0, 2, 1))


def strided(field, tap):
    return field[:, tap // 4 :: 2, tap // 2 % 2 :: 2, tap % 2 :: 2]


def parity(field):
    chans, depth, height, width = field.shape
    return field.reshape(chans, depth // 2, 2, height // 2, 2, width // 2, 2)


def unparity(cube):
    shape = cube.shape
    return cube.reshape(shape[0], shape[1] * 2, shape[3] * 2, shape[5] * 2)


def alternate(parts):
    chans, depth, height, width = parts.shape[1:]
    return (
        parts.reshape(2, 2, 2, chans, depth, height, width)
        .transpose(3, 4, 0, 5, 1, 6, 2)
        .reshape(chans, 2 * depth, 2 * height, 2 * width)
    )


def local(
    tile_image, tile_target, owner_counts, tile_list, w_in, w_res, w_down, w_mid, w_up, head_weight
):
    single_float = jnp.float32
    brain_float_half = jnp.bfloat16
    ranks = lax.axis_size("xy")
    layers = lax.axis_size("gz")
    column = lax.axis_index("xy")
    slots = tile_list.shape[2]
    depth, height, width = (tile_image.shape[3], tile_image.shape[4], tile_image.shape[5])
    per_dev = TPD
    total_tiles = ranks * per_dev
    slot_list = tile_list[0, 0]
    live = jnp.arange(slots) < owner_counts[0, 0]
    select = ((slot_list[None, :] == jnp.arange(total_tiles)[:, None]) & live[None, :]).astype(
        brain_float_half
    )
    payload = jnp.concatenate([tile_image[0, 0][:, None], tile_target[0, 0]], axis=1)
    outgoing = jnp.einsum("ps,sazyx->pazyx", select, payload, preferred_element_type=single_float)
    outgoing = outgoing.astype(brain_float_half).reshape((ranks, per_dev) + payload.shape[1:])
    incoming = lax.all_to_all(outgoing, "xy", 0, 0, tiled=True)
    mine = jnp.sum(incoming.astype(single_float), axis=0).astype(brain_float_half)
    mine_img = mine[:, 0]
    mine_tgt = mine[:, 1:]
    image = mine_img.transpose(1, 2, 0, 3).reshape(1, depth, height, per_dev * width)
    target = mine_tgt.transpose(1, 2, 3, 0, 4).reshape(3, depth, height, per_dev * width)
    voxel_cells = depth * height * per_dev * width * ranks * layers
    block_z = lax.axis_index("gz") * depth
    block_x = column * per_dev * width
    image_wide = with_halo(image, (("gz", 1), ("xy", 3)), 4)
    image_wide = jnp.pad(image_wide, ((0, 0), (0, 0), (1, 1), (0, 0)))
    image_pad = image_wide[:, 3:-3, :, 3:-3]
    h0_wide = jax.nn.relu(convolve(image_wide, w_in[:, :, None]))
    h0_wide = jnp.where(
        inside(h0_wide.shape, block_z - 3, block_x - 3, depth * layers, per_dev * width * ranks),
        h0_wide,
        0.0,
    ).astype(brain_float_half)
    h0_wide = jnp.pad(h0_wide, ((0, 0), (0, 0), (1, 1), (0, 0)))
    h0 = h0_wide[:, 3:-3, 1:-1, 3:-3]
    h0_pad = h0_wide[:, 2:-2, :, 2:-2]
    h1_wide = jax.nn.relu(
        h0_wide[:, 1:-1, 1:-1, 1:-1].astype(single_float) + convolve(h0_wide, w_res)
    ).astype(brain_float_half)
    h1 = h1_wide[:, 2:-2, :, 2:-2]
    down_cube = w_down.reshape((2, 2, 2) + w_down.shape[1:])
    up_cube = w_up.reshape((2, 2, 2) + w_up.shape[1:])
    down_sum = jnp.einsum(
        "abeoc,czaybxe->ozyx", down_cube, parity(h1_wide), preferred_element_type=single_float
    )
    d_wide = jnp.where(
        inside(
            down_sum.shape,
            block_z // 2 - 1,
            block_x // 2 - 1,
            depth * layers // 2,
            per_dev * width * ranks // 2,
        ),
        jax.nn.relu(down_sum),
        0.0,
    ).astype(brain_float_half)
    dfield = d_wide[:, 1:-1, :, 1:-1]
    dfield_pad = jnp.pad(d_wide, ((0, 0), (0, 0), (1, 1), (0, 0)))
    cfield = jax.nn.relu(dfield.astype(single_float) + convolve(dfield_pad, w_mid)).astype(
        brain_float_half
    )
    upward = unparity(
        jnp.einsum("abeoc,czyx->ozaybxe", up_cube, cfield, preferred_element_type=single_float)
    )
    signal_field = jax.nn.relu(h1.astype(single_float) + upward).astype(brain_float_half)
    logits = jnp.einsum(
        "ac,czyx->azyx", head_weight, signal_field, preferred_element_type=single_float
    )
    affinity_map = jax.nn.sigmoid(logits)
    error_field = affinity_map - target.astype(single_float)
    err_out = error_field.astype(brain_float_half)
    err_local = err_out.reshape(3, depth, height, per_dev, width).transpose(3, 0, 1, 2, 4)
    sending = jnp.broadcast_to(err_local[None], (ranks,) + err_local.shape)
    returned = lax.all_to_all(sending, "xy", split_axis=0, concat_axis=0, tiled=True)
    returned = returned.reshape((total_tiles, 3, depth, height, width))
    err_tiles = jnp.einsum(
        "ps,pazyx->sazyx", select, returned, preferred_element_type=single_float
    ).astype(brain_float_half)[None, None]
    logit_gradient = (error_field * affinity_map * (1.0 - affinity_map) / voxel_cells).astype(
        brain_float_half
    )
    head_weight_gradient = jnp.einsum(
        "mtnq,btnq->mb", logit_gradient, signal_field, preferred_element_type=single_float
    )
    gradient_total = jnp.einsum(
        "jn,jbrq->nbrq", head_weight, logit_gradient, preferred_element_type=single_float
    )
    gsf = jnp.where(signal_field > 0, gradient_total, 0.0).astype(brain_float_half)
    gs_cube = parity(gsf)
    grad_up = jnp.einsum(
        "ozaybxe,czyx->abeoc", gs_cube, cfield, preferred_element_type=single_float
    ).reshape(w_up.shape)
    gcoarse = jnp.einsum("abeoc,ozaybxe->czyx", up_cube, gs_cube, preferred_element_type=single_float)
    gquad = jnp.where(cfield > 0, gcoarse, 0.0).astype(brain_float_half)
    grad_mid = tap_grads(gquad, dfield_pad)
    gdown = gquad.astype(single_float) + convolve(framed(gquad), flipped(w_mid))
    gdd = jnp.where(dfield > 0, gdown, 0.0).astype(brain_float_half)
    grad_down = jnp.einsum(
        "ozyx,czaybxe->abeoc", gdd, parity(h1), preferred_element_type=single_float
    ).reshape(w_down.shape)
    spread = unparity(
        jnp.einsum("abeoc,ozyx->czaybxe", down_cube, gdd, preferred_element_type=single_float)
    )
    gres = jnp.where(h1 > 0, gsf.astype(single_float) + spread, 0.0).astype(brain_float_half)
    grad_res = tap_grads(gres, h0_pad)
    gfirst = gres.astype(single_float) + convolve(framed(gres), flipped(w_res))
    gact = jnp.where(h0 > 0, gfirst, 0.0).astype(brain_float_half)
    grad_in = tap_grads(gact, image_pad)[:, :, 0]
    early = tree_sum((grad_down, grad_mid, grad_up, head_weight_gradient), ("gz", "xy"))
    late = tree_sum((grad_in, grad_res), ("gz", "xy"))
    return (err_tiles, late[0], late[1], early[0], early[1], early[2], early[3])


def solution(mesh):
    return jax.shard_map(
        local,
        mesh=mesh,
        in_specs=(
            P("gz", "xy", None, None, None, None),
            P("gz", "xy", None, None, None, None, None),
            P("gz", "xy"),
            P("gz", "xy", None),
            P(),
            P(),
            P(),
            P(),
            P(),
            P(),
        ),
        out_specs=(P("gz", "xy", None, None, None, None, None), P(), P(), P(), P(), P(), P()),
        check_vma=False,
    )
```

```python
import jax
import jax.numpy as jnp
from jax import lax
from jax.sharding import PartitionSpec as P

TPD = 2


def tree_sum(grads, axes):
    count = 1
    for axis in axes:
        count *= lax.axis_size(axis)
    if count & (count - 1):
        return lax.psum(grads, axes)
    flat = jnp.concatenate([g.reshape(-1) for g in grads])
    size = flat.shape[0]
    padded = -(-size // count) * count
    flat = jnp.pad(flat, (0, padded - size))
    index = lax.axis_index(axes[0])
    for axis in axes[1:]:
        index = index * lax.axis_size(axis) + lax.axis_index(axis)
    cur = flat
    step = 1
    while step < count:
        half = cur.shape[0] // 2
        upper = (index // step) % 2 == 1
        low, high = cur[:half], cur[half:]
        keep = jnp.where(upper, high, low)
        send = jnp.where(upper, low, high)
        pairs = [(i, i ^ step) for i in range(count)]
        cur = keep + lax.ppermute(send, axes, pairs)
        step *= 2
    step = count // 2
    while step >= 1:
        pairs = [(i, i ^ step) for i in range(count)]
        other = lax.ppermute(cur, axes, pairs)
        upper = (index // step) % 2 == 1
        cur = jnp.where(upper, jnp.concatenate([other, cur]), jnp.concatenate([cur, other]))
        step //= 2
    out = []
    offset = 0
    for g in grads:
        out.append(cur[offset : offset + g.size].reshape(g.shape))
        offset += g.size
    return tuple(out)


def inside(shape, first_z, first_x, total_z, total_x):
    zs = first_z + jnp.arange(shape[1])
    xs = first_x + jnp.arange(shape[3])
    keep_z = (zs >= 0) & (zs < total_z)
    keep_x = (xs >= 0) & (xs < total_x)
    return (keep_z[:, None] & keep_x[None, :])[None, :, None, :]


def with_halo(cells, sides, width):
    for axis, dim in sides:
        count = lax.axis_size(axis)
        ends = count - 1
        head = lax.slice_in_dim(cells, 0, width, axis=dim)
        tail = lax.slice_in_dim(cells, cells.shape[dim] - width, cells.shape[dim], axis=dim)
        cells = jnp.concatenate(
            [
                lax.ppermute(tail, axis, [(i, (i + 1) % count) for i in range(ends)]),
                cells,
                lax.ppermute(head, axis, [((i + 1) % count, i) for i in range(ends)]),
            ],
            axis=dim,
        )
    return cells


def framed(field):
    padded = with_halo(field, (("gz", 1), ("xy", 3)), 1)
    return jnp.pad(padded, ((0, 0), (0, 0), (1, 1), (0, 0)))


def windows(padded):
    depth = padded.shape[1] - 2
    height = padded.shape[2] - 2
    width = padded.shape[3] - 2
    cols = []
    for tap in range(27):
        off_z, off_y, off_x = (tap // 9, tap // 3 % 3, tap % 3)
        cols.append(
            padded[:, off_z : off_z + depth, off_y : off_y + height, off_x : off_x + width]
        )
    return jnp.stack(cols)


def convolve(padded, weights):
    return jnp.einsum(
        "toc,tczyx->ozyx", weights, windows(padded), preferred_element_type=jnp.float32
    )


def tap_grads(grad, padded):
    return jnp.einsum(
        "ozyx,tczyx->toc", grad, windows(padded), preferred_element_type=jnp.float32
    )


def flipped(weights):
    return jnp.transpose(weights[::-1], (0, 2, 1))


def strided(field, tap):
    return field[:, tap // 4 :: 2, tap // 2 % 2 :: 2, tap % 2 :: 2]


def parity(field):
    chans, depth, height, width = field.shape
    return field.reshape(chans, depth // 2, 2, height // 2, 2, width // 2, 2)


def unparity(cube):
    shape = cube.shape
    return cube.reshape(shape[0], shape[1] * 2, shape[3] * 2, shape[5] * 2)


def alternate(parts):
    chans, depth, height, width = parts.shape[1:]
    return (
        parts.reshape(2, 2, 2, chans, depth, height, width)
        .transpose(3, 4, 0, 5, 1, 6, 2)
        .reshape(chans, 2 * depth, 2 * height, 2 * width)
    )


def local(
    tile_image, tile_target, owner_counts, tile_list, w_in, w_res, w_down, w_mid, w_up, head_weight
):
    single_float = jnp.float32
    brain_float_half = jnp.bfloat16
    ranks = lax.axis_size("xy")
    layers = lax.axis_size("gz")
    column = lax.axis_index("xy")
    slots = tile_list.shape[2]
    depth, height, width = (tile_image.shape[3], tile_image.shape[4], tile_image.shape[5])
    per_dev = TPD
    total_tiles = ranks * per_dev
    slot_list = tile_list[0, 0]
    live = jnp.arange(slots) < owner_counts[0, 0]
    select = ((slot_list[None, :] == jnp.arange(total_tiles)[:, None]) & live[None, :]).astype(
        brain_float_half
    )
    payload = jnp.concatenate([tile_image[0, 0][:, None], tile_target[0, 0]], axis=1)
    outgoing = jnp.einsum("ps,sazyx->pazyx", select, payload, preferred_element_type=single_float)
    outgoing = outgoing.astype(brain_float_half).reshape((ranks, per_dev * payload.shape[1]) + payload.shape[2:])
    first_pos = jnp.arange(ranks) * per_dev
    beside = jnp.stack([first_pos - 1, first_pos + per_dev], axis=1)
    near = ((slot_list[None, None, :] == beside[:, :, None]) & live[None, None, :]).astype(
        brain_float_half
    )
    flank = jnp.einsum("dks,szyx->dkzyx", near, tile_image[0, 0], preferred_element_type=single_float)
    outgoing = jnp.concatenate([outgoing, flank.astype(brain_float_half)], axis=1)
    incoming = lax.all_to_all(outgoing, "xy", 0, 0, tiled=True)
    mine = jnp.sum(incoming.astype(single_float), axis=0).astype(brain_float_half)
    flank_left = mine[per_dev * payload.shape[1]][None, :, :, width - 4 :]
    flank_right = mine[per_dev * payload.shape[1] + 1][None, :, :, :4]
    mine = mine[: per_dev * payload.shape[1]].reshape((per_dev,) + payload.shape[1:])
    mine_img = mine[:, 0]
    mine_tgt = mine[:, 1:]
    image = mine_img.transpose(1, 2, 0, 3).reshape(1, depth, height, per_dev * width)
    target = mine_tgt.transpose(1, 2, 3, 0, 4).reshape(3, depth, height, per_dev * width)
    voxel_cells = depth * height * per_dev * width * ranks * layers
    block_z = lax.axis_index("gz") * depth
    block_x = column * per_dev * width
    image_wide = jnp.concatenate([flank_left, image, flank_right], axis=3)
    image_wide = with_halo(image_wide, (("gz", 1),), 4)
    image_wide = jnp.pad(image_wide, ((0, 0), (0, 0), (1, 1), (0, 0)))
    image_pad = image_wide[:, 3:-3, :, 3:-3]
    h0_wide = jax.nn.relu(convolve(image_wide, w_in[:, :, None]))
    h0_wide = jnp.where(
        inside(h0_wide.shape, block_z - 3, block_x - 3, depth * layers, per_dev * width * ranks),
        h0_wide,
        0.0,
    ).astype(brain_float_half)
    h0_wide = jnp.pad(h0_wide, ((0, 0), (0, 0), (1, 1), (0, 0)))
    h0 = h0_wide[:, 3:-3, 1:-1, 3:-3]
    h0_pad = h0_wide[:, 2:-2, :, 2:-2]
    h1_wide = jax.nn.relu(
        h0_wide[:, 1:-1, 1:-1, 1:-1].astype(single_float) + convolve(h0_wide, w_res)
    ).astype(brain_float_half)
    h1 = h1_wide[:, 2:-2, :, 2:-2]
    down_cube = w_down.reshape((2, 2, 2) + w_down.shape[1:])
    up_cube = w_up.reshape((2, 2, 2) + w_up.shape[1:])
    down_sum = jnp.einsum(
        "abeoc,czaybxe->ozyx", down_cube, parity(h1_wide), preferred_element_type=single_float
    )
    d_wide = jnp.where(
        inside(
            down_sum.shape,
            block_z // 2 - 1,
            block_x // 2 - 1,
            depth * layers // 2,
            per_dev * width * ranks // 2,
        ),
        jax.nn.relu(down_sum),
        0.0,
    ).astype(brain_float_half)
    dfield = d_wide[:, 1:-1, :, 1:-1]
    dfield_pad = jnp.pad(d_wide, ((0, 0), (0, 0), (1, 1), (0, 0)))
    cfield = jax.nn.relu(dfield.astype(single_float) + convolve(dfield_pad, w_mid)).astype(
        brain_float_half
    )
    upward = unparity(
        jnp.einsum("abeoc,czyx->ozaybxe", up_cube, cfield, preferred_element_type=single_float)
    )
    signal_field = jax.nn.relu(h1.astype(single_float) + upward).astype(brain_float_half)
    logits = jnp.einsum(
        "ac,czyx->azyx", head_weight, signal_field, preferred_element_type=single_float
    )
    affinity_map = jax.nn.sigmoid(logits)
    error_field = affinity_map - target.astype(single_float)
    err_out = error_field.astype(brain_float_half)
    err_local = err_out.reshape(3, depth, height, per_dev, width).transpose(3, 0, 1, 2, 4)
    sending = jnp.broadcast_to(err_local[None], (ranks,) + err_local.shape)
    returned = lax.all_to_all(sending, "xy", split_axis=0, concat_axis=0, tiled=True)
    returned = returned.reshape((total_tiles, 3, depth, height, width))
    err_tiles = jnp.einsum(
        "ps,pazyx->sazyx", select, returned, preferred_element_type=single_float
    ).astype(brain_float_half)[None, None]
    logit_gradient = (error_field * affinity_map * (1.0 - affinity_map) / voxel_cells).astype(
        brain_float_half
    )
    head_weight_gradient = jnp.einsum(
        "mtnq,btnq->mb", logit_gradient, signal_field, preferred_element_type=single_float
    )
    gradient_total = jnp.einsum(
        "jn,jbrq->nbrq", head_weight, logit_gradient, preferred_element_type=single_float
    )
    gsf = jnp.where(signal_field > 0, gradient_total, 0.0).astype(brain_float_half)
    gs_cube = parity(gsf)
    grad_up = jnp.einsum(
        "ozaybxe,czyx->abeoc", gs_cube, cfield, preferred_element_type=single_float
    ).reshape(w_up.shape)
    gcoarse = jnp.einsum("abeoc,ozaybxe->czyx", up_cube, gs_cube, preferred_element_type=single_float)
    gquad = jnp.where(cfield > 0, gcoarse, 0.0).astype(brain_float_half)
    grad_mid = tap_grads(gquad, dfield_pad)
    gdown = gquad.astype(single_float) + convolve(framed(gquad), flipped(w_mid))
    gdd = jnp.where(dfield > 0, gdown, 0.0).astype(brain_float_half)
    grad_down = jnp.einsum(
        "ozyx,czaybxe->abeoc", gdd, parity(h1), preferred_element_type=single_float
    ).reshape(w_down.shape)
    spread = unparity(
        jnp.einsum("abeoc,ozyx->czaybxe", down_cube, gdd, preferred_element_type=single_float)
    )
    gres = jnp.where(h1 > 0, gsf.astype(single_float) + spread, 0.0).astype(brain_float_half)
    grad_res = tap_grads(gres, h0_pad)
    gfirst = gres.astype(single_float) + convolve(framed(gres), flipped(w_res))
    gact = jnp.where(h0 > 0, gfirst, 0.0).astype(brain_float_half)
    grad_in = tap_grads(gact, image_pad)[:, :, 0]
    early = tree_sum((grad_down, grad_mid, grad_up, head_weight_gradient), ("gz", "xy"))
    late = tree_sum((grad_in, grad_res), ("gz", "xy"))
    return (err_tiles, late[0], late[1], early[0], early[1], early[2], early[3])


def solution(mesh):
    return jax.shard_map(
        local,
        mesh=mesh,
        in_specs=(
            P("gz", "xy", None, None, None, None),
            P("gz", "xy", None, None, None, None, None),
            P("gz", "xy"),
            P("gz", "xy", None),
            P(),
            P(),
            P(),
            P(),
            P(),
            P(),
        ),
        out_specs=(P("gz", "xy", None, None, None, None, None), P(), P(), P(), P(), P(), P()),
        check_vma=False,
    )
```

```python
import jax
import jax.numpy as jnp
from jax import lax
from jax.sharding import PartitionSpec as P

TPD = 2


def tree_sum(grads, axes):
    count = 1
    for axis in axes:
        count *= lax.axis_size(axis)
    if count & (count - 1):
        return lax.psum(grads, axes)
    flat = jnp.concatenate([g.reshape(-1) for g in grads])
    size = flat.shape[0]
    padded = -(-size // count) * count
    flat = jnp.pad(flat, (0, padded - size))
    index = lax.axis_index(axes[0])
    for axis in axes[1:]:
        index = index * lax.axis_size(axis) + lax.axis_index(axis)
    cur = flat
    step = 1
    while step < count:
        half = cur.shape[0] // 2
        upper = (index // step) % 2 == 1
        low, high = cur[:half], cur[half:]
        keep = jnp.where(upper, high, low)
        send = jnp.where(upper, low, high)
        pairs = [(i, i ^ step) for i in range(count)]
        cur = keep + lax.ppermute(send, axes, pairs)
        step *= 2
    step = count // 2
    while step >= 1:
        pairs = [(i, i ^ step) for i in range(count)]
        other = lax.ppermute(cur, axes, pairs)
        upper = (index // step) % 2 == 1
        cur = jnp.where(upper, jnp.concatenate([other, cur]), jnp.concatenate([cur, other]))
        step //= 2
    out = []
    offset = 0
    for g in grads:
        out.append(cur[offset : offset + g.size].reshape(g.shape))
        offset += g.size
    return tuple(out)


def inside(shape, first_z, first_x, total_z, total_x):
    zs = first_z + jnp.arange(shape[1])
    xs = first_x + jnp.arange(shape[3])
    keep_z = (zs >= 0) & (zs < total_z)
    keep_x = (xs >= 0) & (xs < total_x)
    return (keep_z[:, None] & keep_x[None, :])[None, :, None, :]


def with_halo(cells, sides, width):
    for axis, dim in sides:
        count = lax.axis_size(axis)
        ends = count - 1
        head = lax.slice_in_dim(cells, 0, width, axis=dim)
        tail = lax.slice_in_dim(cells, cells.shape[dim] - width, cells.shape[dim], axis=dim)
        cells = jnp.concatenate(
            [
                lax.ppermute(tail, axis, [(i, (i + 1) % count) for i in range(ends)]),
                cells,
                lax.ppermute(head, axis, [((i + 1) % count, i) for i in range(ends)]),
            ],
            axis=dim,
        )
    return cells


def framed(field):
    padded = with_halo(field, (("gz", 1), ("xy", 3)), 1)
    return jnp.pad(padded, ((0, 0), (0, 0), (1, 1), (0, 0)))


def windows(padded):
    depth = padded.shape[1] - 2
    height = padded.shape[2] - 2
    width = padded.shape[3] - 2
    cols = []
    for tap in range(27):
        off_z, off_y, off_x = (tap // 9, tap // 3 % 3, tap % 3)
        cols.append(
            padded[:, off_z : off_z + depth, off_y : off_y + height, off_x : off_x + width]
        )
    return jnp.stack(cols)


def convolve(padded, weights):
    return jnp.einsum(
        "toc,tczyx->ozyx", weights, windows(padded), preferred_element_type=jnp.float32
    )


def tap_grads(grad, padded):
    return jnp.einsum(
        "ozyx,tczyx->toc", grad, windows(padded), preferred_element_type=jnp.float32
    )


def flipped(weights):
    return jnp.transpose(weights[::-1], (0, 2, 1))


def strided(field, tap):
    return field[:, tap // 4 :: 2, tap // 2 % 2 :: 2, tap % 2 :: 2]


def parity(field):
    chans, depth, height, width = field.shape
    return field.reshape(chans, depth // 2, 2, height // 2, 2, width // 2, 2)


def unparity(cube):
    shape = cube.shape
    return cube.reshape(shape[0], shape[1] * 2, shape[3] * 2, shape[5] * 2)


def alternate(parts):
    chans, depth, height, width = parts.shape[1:]
    return (
        parts.reshape(2, 2, 2, chans, depth, height, width)
        .transpose(3, 4, 0, 5, 1, 6, 2)
        .reshape(chans, 2 * depth, 2 * height, 2 * width)
    )


def local(
    tile_image, tile_target, owner_counts, tile_list, w_in, w_res, w_down, w_mid, w_up, head_weight
):
    single_float = jnp.float32
    brain_float_half = jnp.bfloat16
    ranks = lax.axis_size("xy")
    layers = lax.axis_size("gz")
    column = lax.axis_index("xy")
    slots = tile_list.shape[2]
    depth, height, width = (tile_image.shape[3], tile_image.shape[4], tile_image.shape[5])
    per_dev = TPD
    total_tiles = ranks * per_dev
    slot_list = tile_list[0, 0]
    live = jnp.arange(slots) < owner_counts[0, 0]
    select = ((slot_list[None, :] == jnp.arange(total_tiles)[:, None]) & live[None, :]).astype(
        brain_float_half
    )
    payload = jnp.concatenate([tile_image[0, 0][:, None], tile_target[0, 0]], axis=1)
    outgoing = jnp.einsum("ps,sazyx->pazyx", select, payload, preferred_element_type=single_float)
    outgoing = outgoing.astype(brain_float_half).reshape((ranks, per_dev * payload.shape[1]) + payload.shape[2:])
    first_pos = jnp.arange(ranks) * per_dev
    beside = jnp.stack([first_pos - 1, first_pos + per_dev], axis=1)
    near = ((slot_list[None, None, :] == beside[:, :, None]) & live[None, None, :]).astype(
        brain_float_half
    )
    flank = jnp.einsum("dks,szyx->dkzyx", near, tile_image[0, 0], preferred_element_type=single_float)
    outgoing = jnp.concatenate([outgoing, flank.astype(brain_float_half)], axis=1)
    incoming = lax.all_to_all(outgoing, "xy", 0, 0, tiled=True)
    mine = jnp.sum(incoming.astype(single_float), axis=0).astype(brain_float_half)
    flank_left = mine[per_dev * payload.shape[1]][None, :, :, width - 4 :]
    flank_right = mine[per_dev * payload.shape[1] + 1][None, :, :, :4]
    mine = mine[: per_dev * payload.shape[1]].reshape((per_dev,) + payload.shape[1:])
    mine_img = mine[:, 0]
    mine_tgt = mine[:, 1:]
    image = mine_img.transpose(1, 2, 0, 3).reshape(1, depth, height, per_dev * width)
    target = mine_tgt.transpose(1, 2, 3, 0, 4).reshape(3, depth, height, per_dev * width)
    voxel_cells = depth * height * per_dev * width * ranks * layers
    block_z = lax.axis_index("gz") * depth
    block_x = column * per_dev * width
    image_wide = jnp.concatenate([flank_left, image, flank_right], axis=3)
    image_wide = with_halo(image_wide, (("gz", 1),), 4)
    image_wide = jnp.pad(image_wide, ((0, 0), (0, 0), (1, 1), (0, 0)))
    image_pad = image_wide[:, 3:-3, :, 3:-3]
    h0_wide = jax.nn.relu(convolve(image_wide, w_in[:, :, None]))
    h0_wide = jnp.where(
        inside(h0_wide.shape, block_z - 3, block_x - 3, depth * layers, per_dev * width * ranks),
        h0_wide,
        0.0,
    ).astype(brain_float_half)
    h0_wide = jnp.pad(h0_wide, ((0, 0), (0, 0), (1, 1), (0, 0)))
    h0 = h0_wide[:, 3:-3, 1:-1, 3:-3]
    h0_pad = h0_wide[:, 2:-2, :, 2:-2]
    h0_cols = windows(h0_wide)
    h1_wide = jax.nn.relu(
        h0_wide[:, 1:-1, 1:-1, 1:-1].astype(single_float) + jnp.einsum(
            "toc,tczyx->ozyx", w_res, h0_cols, preferred_element_type=single_float
        )
    ).astype(brain_float_half)
    h1 = h1_wide[:, 2:-2, :, 2:-2]
    down_cube = w_down.reshape((2, 2, 2) + w_down.shape[1:])
    up_cube = w_up.reshape((2, 2, 2) + w_up.shape[1:])
    down_sum = jnp.einsum(
        "abeoc,czaybxe->ozyx", down_cube, parity(h1_wide), preferred_element_type=single_float
    )
    d_wide = jnp.where(
        inside(
            down_sum.shape,
            block_z // 2 - 1,
            block_x // 2 - 1,
            depth * layers // 2,
            per_dev * width * ranks // 2,
        ),
        jax.nn.relu(down_sum),
        0.0,
    ).astype(brain_float_half)
    dfield = d_wide[:, 1:-1, :, 1:-1]
    dfield_pad = jnp.pad(d_wide, ((0, 0), (0, 0), (1, 1), (0, 0)))
    cfield = jax.nn.relu(dfield.astype(single_float) + convolve(dfield_pad, w_mid)).astype(
        brain_float_half
    )
    upward = unparity(
        jnp.einsum("abeoc,czyx->ozaybxe", up_cube, cfield, preferred_element_type=single_float)
    )
    signal_field = jax.nn.relu(h1.astype(single_float) + upward).astype(brain_float_half)
    logits = jnp.einsum(
        "ac,czyx->azyx", head_weight, signal_field, preferred_element_type=single_float
    )
    affinity_map = jax.nn.sigmoid(logits)
    error_field = affinity_map - target.astype(single_float)
    err_out = error_field.astype(brain_float_half)
    err_local = err_out.reshape(3, depth, height, per_dev, width).transpose(3, 0, 1, 2, 4)
    sending = jnp.broadcast_to(err_local[None], (ranks,) + err_local.shape)
    returned = lax.all_to_all(sending, "xy", split_axis=0, concat_axis=0, tiled=True)
    returned = returned.reshape((total_tiles, 3, depth, height, width))
    err_tiles = jnp.einsum(
        "ps,pazyx->sazyx", select, returned, preferred_element_type=single_float
    ).astype(brain_float_half)[None, None]
    logit_gradient = (error_field * affinity_map * (1.0 - affinity_map) / voxel_cells).astype(
        brain_float_half
    )
    head_weight_gradient = jnp.einsum(
        "mtnq,btnq->mb", logit_gradient, signal_field, preferred_element_type=single_float
    )
    gradient_total = jnp.einsum(
        "jn,jbrq->nbrq", head_weight, logit_gradient, preferred_element_type=single_float
    )
    gsf = jnp.where(signal_field > 0, gradient_total, 0.0).astype(brain_float_half)
    gs_cube = parity(gsf)
    grad_up = jnp.einsum(
        "ozaybxe,czyx->abeoc", gs_cube, cfield, preferred_element_type=single_float
    ).reshape(w_up.shape)
    gcoarse = jnp.einsum("abeoc,ozaybxe->czyx", up_cube, gs_cube, preferred_element_type=single_float)
    gquad = jnp.where(cfield > 0, gcoarse, 0.0).astype(brain_float_half)
    grad_mid = tap_grads(gquad, dfield_pad)
    gdown = gquad.astype(single_float) + convolve(framed(gquad), flipped(w_mid))
    gdd = jnp.where(dfield > 0, gdown, 0.0).astype(brain_float_half)
    grad_down = jnp.einsum(
        "ozyx,czaybxe->abeoc", gdd, parity(h1), preferred_element_type=single_float
    ).reshape(w_down.shape)
    spread = unparity(
        jnp.einsum("abeoc,ozyx->czaybxe", down_cube, gdd, preferred_element_type=single_float)
    )
    gres = jnp.where(h1 > 0, gsf.astype(single_float) + spread, 0.0).astype(brain_float_half)
    grad_res = jnp.einsum(
        "ozyx,tczyx->toc",
        gres,
        h0_cols[:, :, 2:-2, :, 2:-2],
        preferred_element_type=single_float,
    )
    gfirst = gres.astype(single_float) + convolve(framed(gres), flipped(w_res))
    gact = jnp.where(h0 > 0, gfirst, 0.0).astype(brain_float_half)
    grad_in = tap_grads(gact, image_pad)[:, :, 0]
    early = tree_sum((grad_down, grad_mid, grad_up, head_weight_gradient), ("gz", "xy"))
    late = tree_sum((grad_in, grad_res), ("gz", "xy"))
    return (err_tiles, late[0], late[1], early[0], early[1], early[2], early[3])


def solution(mesh):
    return jax.shard_map(
        local,
        mesh=mesh,
        in_specs=(
            P("gz", "xy", None, None, None, None),
            P("gz", "xy", None, None, None, None, None),
            P("gz", "xy"),
            P("gz", "xy", None),
            P(),
            P(),
            P(),
            P(),
            P(),
            P(),
        ),
        out_specs=(P("gz", "xy", None, None, None, None, None), P(), P(), P(), P(), P(), P()),
        check_vma=False,
    )
```
